128 devices in a mesh: dom: 8 (over y, core), seq: 16 (over x, z).
Axes of the slice: x: 4, y: 4, z: 4, core: 2. Of those that a mesh axis runs over, the one named last changes fastest.
Arguments:
- tokens_x: bfloat16 [32768, 4096], P(('dom', 'seq')), may hold values from -6 to 6
- gate_z: bfloat16 [32768, 4096], P(('dom', 'seq')), may hold values from -6 to 6
- in_b: bfloat16 [32768, 128], P(('dom', 'seq')), may hold values from -6 to 6
- in_c: bfloat16 [32768, 128], P(('dom', 'seq')), may hold values from -0.19921875 to 0.19921875
- log_decay: bfloat16 [32768, 64], P(('dom', 'seq')), may hold values from -1 to 0
- domain_ids: int32 [8, 16, 8], P('dom', 'seq'), may hold values from 0 to 7, each once within a row
- out_weight: bfloat16 [8, 4096, 4096], P('dom', None, 'seq'), may hold values from -0.09375 to 0.09375
- norm_gain: float32 [8, 4096], P('dom'), may hold values from 0.1 to 1.9
- skip_gain: float32 [8, 64], P('dom'), may hold values from 0.5 to 8
Outputs:
- mixed: bfloat16 [8, 4096, 4096], P('dom', 'seq')
The draws below stay inside these ranges and needn't reach their ends.
Inputs may be any that keep to these rules, and one draw needn't show every extreme that they name: Each row of domain_ids names every domain once.
All inputs are finite; a program needn't handle non-finite values.
Results may differ from the reference program's by a relative error of at most 0.0056.
Values may be sent and summed in bfloat16 or wider, within the bound.
No kernel may reach another device: no remote copies, remote signals or barrier semaphores. Data moves between devices by JAX's collectives and lax.ppermute only.
A program may use at most 192 MiB of HBM per device.

```python
import math
import jax
import jax.numpy as jnp
from jax import lax

D = 4096
HALF_HEADS = 64
P_SIZE = 64
N = 128
SPAN = 256
TOK_DEV = 256
HP = 4096
SEG = 32
DOMAIN_TOKENS = 4096
TOTAL_TOKENS = 32768
N_DOM = 8
N_SEQ = 16


def draw_log_decay(key, part):
    key_rows = jax.random.split(key, 7)
    fast_share = 0.5
    fast = jax.random.uniform(key_rows[0], (HALF_HEADS,)) < fast_share
    fast_rate = jnp.exp(jax.random.uniform(key_rows[1], (HALF_HEADS,), minval=jnp.log(1.0 / 50.0), maxval=jnp.log(1.0 / 25.0)))
    slow_rate = jax.random.uniform(key_rows[2], (HALF_HEADS,), minval=0.1, maxval=0.6) * 2.302585 / DOMAIN_TOKENS
    decay_speed = jnp.where(fast, fast_rate, slow_rate)
    accelerator_multiple = jnp.exp(jax.random.uniform(key_rows[3], (TOTAL_TOKENS // TOK_DEV, 1), minval=-0.5, maxval=0.4))
    accelerator_multiple = jnp.repeat(accelerator_multiple, TOK_DEV, axis=0)
    approximate_value = jax.random.uniform(key_rows[4], (TOTAL_TOKENS, HALF_HEADS), minval=0.5, maxval=1.5)
    token_group = jax.random.uniform(key_rows[5], (TOTAL_TOKENS, 1)) < 3.0 / DOMAIN_TOKENS
    group_length = jnp.log(jax.random.uniform(key_rows[6], (TOTAL_TOKENS, HALF_HEADS), minval=0.5, maxval=0.8))
    value_rows = -decay_speed[None, :] * accelerator_multiple * approximate_value + jnp.where(token_group, group_length, 0.0)
    return value_rows.astype(jnp.bfloat16)


def block_scale(rng, dims, cuts, least, largest):
    loudness = 1.0
    for axis_at, parts in cuts:
        draws = jax.random.uniform(jax.random.fold_in(jax.random.fold_in(rng, 6), axis_at), (parts,), jnp.float32, least / len(cuts), largest / len(cuts))
        loudness = loudness * jnp.repeat(jnp.exp(draws), dims[axis_at] // parts).reshape((-1,) + (1,) * (len(dims) - 1 - axis_at))
    return loudness


def noise(rng, shape, scale, reach, shards=(), kind=jnp.bfloat16):
    values = jax.random.normal(rng, shape, jnp.float32) * scale
    if len(shards) > 0:
        values = block_scale(rng, shape, shards, -0.22, 0.18) * values
    return jnp.clip(values, min=-reach, max=reach).astype(kind)


def setup_inputs(seed: int = 0) -> dict:
    key_list = jax.random.split(jax.random.key(seed), 10)
    return {
        "tokens_x": noise(key_list[0], (TOTAL_TOKENS, HP), 1.0, 6.0, ((0, 128),)),
        "gate_z": noise(key_list[1], (TOTAL_TOKENS, HP), 1.0, 6.0, ((0, 128),)),
        "in_b": noise(key_list[2], (TOTAL_TOKENS, N), 1.0, 6.0, ((0, 128),)),
        "in_c": noise(key_list[3], (TOTAL_TOKENS, N), 0.03, 0.19921875, ((0, 128),)),
        "log_decay": draw_log_decay(jax.random.fold_in(key_list[9], 71), 0),
        "domain_ids": jax.vmap(lambda own: jax.random.permutation(own, N_DOM))(jax.random.split(key_list[5], N_DOM * N_SEQ)).reshape((N_DOM, N_SEQ, N_DOM)).astype(jnp.int32),
        "out_weight": noise(key_list[6], (N_DOM, HP, D), HP ** -0.5, 0.09375, ((0, 8), (2, 16))),
        "norm_gain": jnp.clip(1.0 + 0.18 * jax.random.normal(key_list[7], (N_DOM, HP), jnp.float32), 0.1, 1.9),
        "skip_gain": jnp.clip(jnp.exp(math.log(8.0) - 2.7725887 * jax.random.uniform(key_list[8], (N_DOM, HALF_HEADS), jnp.float32) ** block_scale(key_list[8], (N_DOM, HALF_HEADS), ((0, 8),), -0.2, 0.2)), 0.5, 8.0),
    }


def stream_order(arr, order):
    width = arr.shape[-1]
    blocks = arr.reshape(N_DOM, N_SEQ, N_DOM, SEG, width)
    picked = jnp.take_along_axis(blocks, order[:, :, :, None, None], axis=2)
    return jnp.transpose(picked, (2, 1, 0, 3, 4)).reshape(N_DOM, DOMAIN_TOKENS, width)

def one_domain(packed):
    xs, zs, bs, cs, ls, weight, gain, skip = packed
    blocks = DOMAIN_TOKENS // SPAN
    xc = xs.reshape(blocks, SPAN, HALF_HEADS, P_SIZE)
    zc = zs.reshape(blocks, SPAN, HP)
    bc = bs.reshape(blocks, SPAN, N)
    cc = cs.reshape(blocks, SPAN, N)
    lc = ls.astype(jnp.float32).reshape(blocks, SPAN, HALF_HEADS)
    rows = jnp.arange(SPAN)
    lower = rows[:, None] >= rows[None, :]

    def step(state, inputs):
        xk, zk, bk, ck, lk = inputs
        cum = jnp.cumsum(lk, axis=0)
        scores = jnp.dot(ck, bk.T, preferred_element_type=jnp.float32)
        diff = cum[:, None, :] - cum[None, :, :]
        decay = jnp.where(lower[:, :, None], jnp.exp(jnp.minimum(diff, 0.0)), 0.0)
        weights = (scores[:, :, None] * decay).astype(jnp.bfloat16)
        inner = jnp.einsum('tuh,uhp->thp', weights.astype(jnp.float32), xk.astype(jnp.float32))
        carried = jnp.einsum('tn,hpn->thp', ck.astype(jnp.float32), state, precision=lax.Precision.HIGHEST)
        ys = inner + jnp.exp(cum)[:, :, None] * carried + skip[None, :, None] * xk.astype(jnp.float32)
        decayed = (xk.astype(jnp.float32) * jnp.exp(cum[-1][None, :] - cum)[:, :, None]).astype(jnp.bfloat16)
        block_state = jnp.einsum('uhp,un->hpn', decayed.astype(jnp.float32), bk.astype(jnp.float32))
        new_state = jnp.exp(cum[-1])[:, None, None] * state + block_state
        gated = ys.reshape(SPAN, HP) * jax.nn.silu(zk.astype(jnp.float32))
        normed = (gated * lax.rsqrt(lax.optimization_barrier(jnp.mean(gated * gated, axis=-1, keepdims=True)) + 1e-05) * gain[None, :]).astype(jnp.bfloat16)
        out = jnp.dot(normed, weight, preferred_element_type=jnp.float32).astype(jnp.bfloat16)
        return (new_state, out)
    start = jnp.zeros((HALF_HEADS, P_SIZE, N), jnp.float32)
    _, outs = lax.scan(step, start, (xc, zc, bc, cc, lc))
    return outs.reshape(DOMAIN_TOKENS, D)

def reference(tokens_x, gate_z, in_b, in_c, log_decay, domain_ids, out_weight, norm_gain, skip_gain):
    order = jnp.argsort(domain_ids, axis=-1).astype(jnp.int32)
    xs = stream_order(tokens_x, order)
    zs = stream_order(gate_z, order)
    bs = stream_order(in_b, order)
    cs = stream_order(in_c, order)
    ls = stream_order(log_decay, order)
    return lax.map(one_domain, (xs, zs, bs, cs, ls, out_weight, norm_gain, skip_gain))
```

```python
import jax
import jax.numpy as jnp
from jax import lax
from jax.sharding import PartitionSpec as P

SPAN = 256


def shifted(block, axis, distance):
    devices = range(lax.axis_size(axis))
    route = [(i - distance, i) for i in devices if i - distance in devices]
    return lax.ppermute(block, axis, route)


def per_device(
    tokens_x, gate_z, in_b, in_c, log_decay, domain_ids, out_weight, norm_gain, skip_gain
):
    groups = lax.axis_size("dom")
    rows = tokens_x.shape[0]
    seg_rows = rows // groups
    order = jnp.argsort(domain_ids.reshape(groups))

    def arrange(value_rows):
        return jnp.take(value_rows.reshape(groups, seg_rows, value_rows.shape[-1]), order, axis=0)

    received = (
        lax.all_to_all(arrange(tokens_x), "dom", split_axis=0, concat_axis=0, tiled=True),
        lax.all_to_all(arrange(gate_z), "dom", split_axis=0, concat_axis=0, tiled=True),
        lax.all_to_all(arrange(in_b), "dom", split_axis=0, concat_axis=0, tiled=True),
        lax.all_to_all(arrange(in_c), "dom", split_axis=0, concat_axis=0, tiled=True),
        lax.all_to_all(arrange(log_decay), "dom", split_axis=0, concat_axis=0, tiled=True),
    )
    xs, zs, bs, cs, ls = [piece.reshape(rows, piece.shape[-1]) for piece in received]
    heads = skip_gain.shape[-1]
    width = xs.shape[1]
    hsize = width // heads
    nstate = bs.shape[1]
    blocks = rows // SPAN
    xc = xs.reshape(blocks, SPAN, heads, hsize)
    bc = bs.reshape(blocks, SPAN, nstate)
    cc = cs.reshape(blocks, SPAN, nstate)
    cum = jnp.cumsum(ls.astype(jnp.float32).reshape(blocks, SPAN, heads), axis=1)
    scores = jnp.einsum("cin,cjn->cij", cc, bc, preferred_element_type=jnp.float32)
    cum_heads = jnp.transpose(cum, (0, 2, 1))
    diff = cum_heads[:, :, :, None] - cum_heads[:, :, None, :]
    positions = jnp.arange(SPAN)
    lower = positions[:, None] >= positions[None, :]
    decay = jnp.where(lower[None, None], jnp.exp(jnp.minimum(diff, 0.0)), 0.0)
    weights = (scores[:, None] * decay).astype(jnp.bfloat16)
    inner = jnp.einsum("chij,cjhp->cihp", weights, xc, preferred_element_type=jnp.float32)
    totals = cum[:, -1, :]
    decayed = (xc.astype(jnp.float32) * jnp.exp(totals[:, None, :] - cum)[..., None]).astype(
        jnp.bfloat16
    )
    block_state = jnp.einsum("cjhp,cjn->chpn", decayed, bc, preferred_element_type=jnp.float32)
    running = jnp.zeros((heads, hsize, nstate), jnp.float32)
    before = [running]
    running = jnp.exp(totals[0])[:, None, None] * running + block_state[0]
    local_end = running
    local_before = jnp.stack(before, axis=0)
    shard_decay = jnp.exp(jnp.sum(totals, axis=0))
    packed = jnp.concatenate(
        [local_end, jnp.broadcast_to(shard_decay[None, :, None], (1, heads, nstate))], axis=0
    )
    packed = shifted(packed, "seq", 1)
    distance = 1
    while distance < lax.axis_size("seq"):
        got = shifted(packed, "seq", distance)
        scale = packed[heads:]
        packed = jnp.concatenate(
            [jnp.transpose(scale, (1, 0, 2))[:, :, :1] * got[:heads] + packed[:heads], scale * got[heads:]],
            axis=0,
        )
        distance *= 2
    incoming = packed[:heads]
    prefix = jnp.cumsum(totals, axis=0) - totals
    full_before = local_before + jnp.exp(prefix)[:, :, None, None] * incoming[None]
    carried = jnp.einsum(
        "cin,chpn->cihp", cc.astype(jnp.float32), full_before, precision=lax.Precision.HIGHEST
    )
    ys = (
        inner
        + jnp.exp(cum)[..., None] * carried
        + skip_gain[0][None, None, :, None] * xc.astype(jnp.float32)
    )
    gated = ys.reshape(rows, width) * jax.nn.silu(zs.astype(jnp.float32))
    normed = (
        gated
        * lax.rsqrt(jnp.mean(gated * gated, axis=-1, keepdims=True) + 1e-05)
        * norm_gain[0][None, :]
    ).astype(jnp.bfloat16)
    mixed = jnp.dot(
        normed,
        lax.all_gather(out_weight[0], "seq", axis=1, tiled=True),
        preferred_element_type=jnp.float32,
    ).astype(jnp.bfloat16)
    return mixed.reshape(1, rows, mixed.shape[-1])


def solution(mesh):
    in_specs = (
        P(("dom", "seq"), None),
        P(("dom", "seq"), None),
        P(("dom", "seq"), None),
        P(("dom", "seq"), None),
        P(("dom", "seq"), None),
        P("dom", "seq", None),
        P("dom", None, "seq"),
        P("dom", None),
        P("dom", None),
    )
    out_specs = P("dom", "seq", None)
    return jax.shard_map(
        per_device, mesh=mesh, in_specs=in_specs, out_specs=out_specs, check_vma=False
    )
```

```python
import jax
import jax.numpy as jnp
from jax import lax
from jax.sharding import PartitionSpec as P

SPAN = 256


def per_device(
    tokens_x, gate_z, in_b, in_c, log_decay, domain_ids, out_weight, norm_gain, skip_gain
):
    groups = lax.axis_size("dom")
    shards = lax.axis_size("seq")
    rows = tokens_x.shape[0]
    seg_rows = rows // groups
    width = tokens_x.shape[1]
    nstate = in_b.shape[1]
    heads = skip_gain.shape[-1]
    hsize = width // heads
    order = jnp.argsort(domain_ids.reshape(groups))

    pad = (-log_decay.shape[1]) % 128
    packed = jnp.concatenate(
        [tokens_x, gate_z, in_b, in_c, log_decay, jnp.zeros((rows, pad), log_decay.dtype)], axis=1
    )
    packed = jnp.take(packed.reshape(groups, seg_rows, packed.shape[-1]), order, axis=0)
    packed = lax.all_to_all(packed, "dom", split_axis=0, concat_axis=0, tiled=True)
    packed = packed.reshape(rows, packed.shape[-1])
    xs = packed[:, :width]
    zs = packed[:, width : 2 * width]
    bs = packed[:, 2 * width : 2 * width + nstate]
    cs = packed[:, 2 * width + nstate : 2 * width + 2 * nstate]
    ls = packed[:, 2 * width + 2 * nstate : 2 * width + 2 * nstate + heads]

    local = width // shards
    lheads = heads // shards
    xbc = jnp.concatenate(
        [
            jnp.transpose(xs.reshape(rows, shards, local), (1, 0, 2)),
            jnp.broadcast_to(bs[None], (shards, rows, nstate)),
            jnp.broadcast_to(cs[None], (shards, rows, nstate)),
        ],
        axis=2,
    )
    xbc = lax.all_to_all(xbc, "seq", split_axis=0, concat_axis=0, tiled=True)
    lsh = jnp.transpose(ls.reshape(rows, shards, lheads), (1, 0, 2))
    lsh = lax.all_to_all(lsh, "seq", split_axis=0, concat_axis=0, tiled=True)

    blocks = shards * rows // SPAN
    xc = xbc[:, :, :local].reshape(blocks, SPAN, lheads, hsize)
    bc = xbc[:, :, local : local + nstate].reshape(blocks, SPAN, nstate)
    cc = xbc[:, :, local + nstate :].reshape(blocks, SPAN, nstate)
    cum = jnp.cumsum(lsh.astype(jnp.float32).reshape(blocks, SPAN, lheads), axis=1)
    scores = jnp.einsum("cin,cjn->cij", cc, bc, preferred_element_type=jnp.float32)
    cum_heads = jnp.transpose(cum, (0, 2, 1))
    diff = cum_heads[:, :, :, None] - cum_heads[:, :, None, :]
    positions = jnp.arange(SPAN)
    lower = positions[:, None] >= positions[None, :]
    decay = jnp.where(lower[None, None], jnp.exp(jnp.minimum(diff, 0.0)), 0.0)
    weights = (scores[:, None] * decay).astype(jnp.bfloat16)
    inner = jnp.einsum("chij,cjhp->cihp", weights, xc, preferred_element_type=jnp.float32)
    totals = cum[:, -1, :]
    decayed = (xc.astype(jnp.float32) * jnp.exp(totals[:, None, :] - cum)[..., None]).astype(
        jnp.bfloat16
    )
    block_state = jnp.einsum("cjhp,cjn->chpn", decayed, bc, preferred_element_type=jnp.float32)

    idx = jnp.arange(blocks)
    between = (idx[None, :, None] < idx[None, None, :]) & (idx[None, None, :] < idx[:, None, None])
    gaps = jnp.einsum(
        "kji,ih->hkj", between.astype(jnp.float32), totals, precision=lax.Precision.HIGHEST
    )
    earlier = idx[None, :] < idx[:, None]
    carry = jnp.where(earlier[None], jnp.exp(jnp.minimum(gaps, 0.0)), 0.0)
    before = jnp.einsum("hkj,jhpn->khpn", carry, block_state, precision=lax.Precision.HIGHEST)
    carried = jnp.einsum(
        "cin,chpn->cihp", cc.astype(jnp.float32), before, precision=lax.Precision.HIGHEST
    )
    skip = lax.dynamic_slice_in_dim(skip_gain[0], lax.axis_index("seq") * lheads, lheads)
    ys = (
        inner
        + jnp.exp(cum)[..., None] * carried
        + skip[None, None, :, None] * xc.astype(jnp.float32)
    )

    ys = lax.all_to_all(
        ys.reshape(shards, rows, local), "seq", split_axis=0, concat_axis=0, tiled=True
    )
    ys = jnp.transpose(ys, (1, 0, 2)).reshape(rows, width)
    gated = ys * jax.nn.silu(zs.astype(jnp.float32))
    normed = (
        gated
        * lax.rsqrt(jnp.mean(gated * gated, axis=-1, keepdims=True) + 1e-05)
        * norm_gain[0][None, :]
    ).astype(jnp.bfloat16)
    mixed = jnp.dot(
        normed,
        lax.all_gather(out_weight[0], "seq", axis=1, tiled=True),
        preferred_element_type=jnp.float32,
    ).astype(jnp.bfloat16)
    return mixed.reshape(1, rows, mixed.shape[-1])


def solution(mesh):
    in_specs = (
        P(("dom", "seq"), None),
        P(("dom", "seq"), None),
        P(("dom", "seq"), None),
        P(("dom", "seq"), None),
        P(("dom", "seq"), None),
        P("dom", "seq", None),
        P("dom", None, "seq"),
        P("dom", None),
        P("dom", None),
    )
    out_specs = P("dom", "seq", None)
    return jax.shard_map(
        per_device, mesh=mesh, in_specs=in_specs, out_specs=out_specs, check_vma=False
    )
```

```python
import jax
import jax.numpy as jnp
from jax import lax
from jax.sharding import PartitionSpec as P

SPAN = 256


def per_device(
    tokens_x, gate_z, in_b, in_c, log_decay, domain_ids, out_weight, norm_gain, skip_gain
):
    groups = lax.axis_size("dom")
    shards = lax.axis_size("seq")
    rows = tokens_x.shape[0]
    seg_rows = rows // groups
    width = tokens_x.shape[1]
    nstate = in_b.shape[1]
    heads = skip_gain.shape[-1]
    hsize = width // heads
    order = jnp.argsort(domain_ids.reshape(groups))

    def arrange(value_rows):
        return jnp.take(value_rows.reshape(groups, seg_rows, value_rows.shape[-1]), order, axis=0)

    pad = (-log_decay.shape[1]) % 128
    packed = jnp.concatenate(
        [tokens_x, in_b, in_c, log_decay, jnp.zeros((rows, pad), log_decay.dtype)], axis=1
    )
    packed = lax.all_to_all(arrange(packed), "dom", split_axis=0, concat_axis=0, tiled=True)
    packed = packed.reshape(rows, packed.shape[-1])
    zs = lax.all_to_all(arrange(gate_z), "dom", split_axis=0, concat_axis=0, tiled=True)
    zs = zs.reshape(rows, width)
    xs = packed[:, :width]
    bs = packed[:, width : width + nstate]
    cs = packed[:, width + nstate : width + 2 * nstate]
    ls = packed[:, width + 2 * nstate : width + 2 * nstate + heads]

    local = width // shards
    lheads = heads // shards
    xbc = jnp.concatenate(
        [
            jnp.transpose(xs.reshape(rows, shards, local), (1, 0, 2)),
            jnp.broadcast_to(bs[None], (shards, rows, nstate)),
            jnp.broadcast_to(cs[None], (shards, rows, nstate)),
        ],
        axis=2,
    )
    xbc = lax.all_to_all(xbc, "seq", split_axis=0, concat_axis=0, tiled=True)
    lsh = jnp.transpose(ls.reshape(rows, shards, lheads), (1, 0, 2))
    lsh = lax.all_to_all(lsh, "seq", split_axis=0, concat_axis=0, tiled=True)

    blocks = shards * rows // SPAN
    xc = xbc[:, :, :local].reshape(blocks, SPAN, lheads, hsize)
    bc = xbc[:, :, local : local + nstate].reshape(blocks, SPAN, nstate)
    cc = xbc[:, :, local + nstate :].reshape(blocks, SPAN, nstate)
    cum = jnp.cumsum(lsh.astype(jnp.float32).reshape(blocks, SPAN, lheads), axis=1)
    scores = jnp.einsum("cin,cjn->cij", cc, bc, preferred_element_type=jnp.float32)
    cum_heads = jnp.transpose(cum, (0, 2, 1))
    diff = cum_heads[:, :, :, None] - cum_heads[:, :, None, :]
    positions = jnp.arange(SPAN)
    lower = positions[:, None] >= positions[None, :]
    decay = jnp.where(lower[None, None], jnp.exp(jnp.minimum(diff, 0.0)), 0.0)
    weights = (scores[:, None] * decay).astype(jnp.bfloat16)
    inner = jnp.einsum("chij,cjhp->cihp", weights, xc, preferred_element_type=jnp.float32)
    totals = cum[:, -1, :]
    decayed = (xc.astype(jnp.float32) * jnp.exp(totals[:, None, :] - cum)[..., None]).astype(
        jnp.bfloat16
    )
    block_state = jnp.einsum("cjhp,cjn->chpn", decayed, bc, preferred_element_type=jnp.float32)

    idx = jnp.arange(blocks)
    between = (idx[None, :, None] < idx[None, None, :]) & (idx[None, None, :] < idx[:, None, None])
    gaps = jnp.einsum(
        "kji,ih->hkj", between.astype(jnp.float32), totals, precision=lax.Precision.HIGHEST
    )
    earlier = idx[None, :] < idx[:, None]
    carry = jnp.where(earlier[None], jnp.exp(jnp.minimum(gaps, 0.0)), 0.0)
    before = jnp.einsum("hkj,jhpn->khpn", carry, block_state, precision=lax.Precision.HIGHEST)
    carried = jnp.einsum(
        "cin,chpn->cihp", cc.astype(jnp.float32), before, precision=lax.Precision.HIGHEST
    )
    skip = lax.dynamic_slice_in_dim(skip_gain[0], lax.axis_index("seq") * lheads, lheads)
    ys = (
        inner
        + jnp.exp(cum)[..., None] * carried
        + skip[None, None, :, None] * xc.astype(jnp.float32)
    )

    ys = lax.all_to_all(
        ys.reshape(shards, rows, local), "seq", split_axis=0, concat_axis=0, tiled=True
    )
    ys = jnp.transpose(ys, (1, 0, 2)).reshape(rows, width)
    gated = ys * jax.nn.silu(zs.astype(jnp.float32))
    normed = (
        gated
        * lax.rsqrt(jnp.mean(gated * gated, axis=-1, keepdims=True) + 1e-05)
        * norm_gain[0][None, :]
    ).astype(jnp.bfloat16)
    pieces = 4
    span = width // pieces
    mixed = None
    for k in range(pieces):
        part = lax.all_gather(out_weight[0, k * span : (k + 1) * span], "seq", axis=1, tiled=True)
        term = jnp.dot(normed[:, k * span : (k + 1) * span], part, preferred_element_type=jnp.float32)
        mixed = term if mixed is None else mixed + term
    mixed = mixed.astype(jnp.bfloat16)
    return mixed.reshape(1, rows, mixed.shape[-1])


def solution(mesh):
    in_specs = (
        P(("dom", "seq"), None),
        P(("dom", "seq"), None),
        P(("dom", "seq"), None),
        P(("dom", "seq"), None),
        P(("dom", "seq"), None),
        P("dom", "seq", None),
        P("dom", None, "seq"),
        P("dom", None),
        P("dom", None),
    )
    out_specs = P("dom", "seq", None)
    return jax.shard_map(
        per_device, mesh=mesh, in_specs=in_specs, out_specs=out_specs, check_vma=False
    )
```

```python
import jax
import jax.numpy as jnp
from jax import lax
from jax.sharding import PartitionSpec as P

SPAN = 256


def per_device(
    tokens_x, gate_z, in_b, in_c, log_decay, domain_ids, out_weight, norm_gain, skip_gain
):
    groups = lax.axis_size("dom")
    shards = lax.axis_size("seq")
    rows = tokens_x.shape[0]
    seg_rows = rows // groups
    width = tokens_x.shape[1]
    nstate = in_b.shape[1]
    heads = skip_gain.shape[-1]
    hsize = width // heads
    order = jnp.argsort(domain_ids.reshape(groups))

    def arrange(value_rows):
        return jnp.take(value_rows.reshape(groups, seg_rows, value_rows.shape[-1]), order, axis=0)

    pad = (-log_decay.shape[1]) % 128
    packed = jnp.concatenate(
        [tokens_x, in_b, in_c, log_decay, jnp.zeros((rows, pad), log_decay.dtype)], axis=1
    )
    packed = lax.all_to_all(arrange(packed), "dom", split_axis=0, concat_axis=0, tiled=True)
    packed = packed.reshape(rows, packed.shape[-1])
    zs = lax.all_to_all(arrange(gate_z), "dom", split_axis=0, concat_axis=0, tiled=True)
    zs = zs.reshape(rows, width)
    xs = packed[:, :width]
    bs = packed[:, width : width + nstate]
    cs = packed[:, width + nstate : width + 2 * nstate]
    ls = packed[:, width + 2 * nstate : width + 2 * nstate + heads]

    local = width // shards
    lheads = heads // shards
    xbc = jnp.concatenate(
        [
            jnp.transpose(xs.reshape(rows, shards, local), (1, 0, 2)),
            jnp.broadcast_to(bs[None], (shards, rows, nstate)),
            jnp.broadcast_to(cs[None], (shards, rows, nstate)),
        ],
        axis=2,
    )
    xbc = lax.all_to_all(xbc, "seq", split_axis=0, concat_axis=0, tiled=True)
    lsh = jnp.transpose(ls.reshape(rows, shards, lheads), (1, 0, 2))
    lsh = lax.all_to_all(lsh, "seq", split_axis=0, concat_axis=0, tiled=True)

    blocks = shards * rows // SPAN
    xc = xbc[:, :, :local].reshape(blocks, SPAN, lheads, hsize)
    bc = xbc[:, :, local : local + nstate].reshape(blocks, SPAN, nstate)
    cc = xbc[:, :, local + nstate :].reshape(blocks, SPAN, nstate)
    cum = jnp.cumsum(lsh.astype(jnp.float32).reshape(blocks, SPAN, lheads), axis=1)
    scores = jnp.einsum("cin,cjn->cij", cc, bc, preferred_element_type=jnp.float32)
    cum_heads = jnp.transpose(cum, (0, 2, 1))
    diff = cum_heads[:, :, :, None] - cum_heads[:, :, None, :]
    positions = jnp.arange(SPAN)
    lower = positions[:, None] >= positions[None, :]
    decay = jnp.where(lower[None, None], jnp.exp(jnp.minimum(diff, 0.0)), 0.0)
    weights = (scores[:, None] * decay).astype(jnp.bfloat16)
    inner = jnp.einsum("chij,cjhp->cihp", weights, xc, preferred_element_type=jnp.float32)
    totals = cum[:, -1, :]
    decayed = (xc.astype(jnp.float32) * jnp.exp(totals[:, None, :] - cum)[..., None]).astype(
        jnp.bfloat16
    )
    block_state = jnp.einsum("cjhp,cjn->chpn", decayed, bc, preferred_element_type=jnp.float32)

    idx = jnp.arange(blocks)
    between = (idx[None, :, None] < idx[None, None, :]) & (idx[None, None, :] < idx[:, None, None])
    gaps = jnp.einsum(
        "kji,ih->hkj", between.astype(jnp.float32), totals, precision=lax.Precision.HIGHEST
    )
    earlier = idx[None, :] < idx[:, None]
    carry = jnp.where(earlier[None], jnp.exp(jnp.minimum(gaps, 0.0)), 0.0)
    before = jnp.einsum("hkj,jhpn->khpn", carry, block_state, precision=lax.Precision.HIGHEST)
    carried = jnp.einsum(
        "cin,chpn->cihp", cc.astype(jnp.float32), before, precision=lax.Precision.HIGHEST
    )
    skip = lax.dynamic_slice_in_dim(skip_gain[0], lax.axis_index("seq") * lheads, lheads)
    ys = (
        inner
        + jnp.exp(cum)[..., None] * carried
        + skip[None, None, :, None] * xc.astype(jnp.float32)
    )

    ys = lax.all_to_all(
        ys.reshape(shards, rows, local), "seq", split_axis=0, concat_axis=0, tiled=True
    )
    ys = jnp.transpose(ys, (1, 0, 2)).reshape(rows, width)
    gated = ys * jax.nn.silu(zs.astype(jnp.float32))
    normed = (
        gated
        * lax.rsqrt(jnp.mean(gated * gated, axis=-1, keepdims=True) + 1e-05)
        * norm_gain[0][None, :]
    ).astype(jnp.bfloat16)
    mixed = jnp.dot(
        normed,
        lax.all_gather(out_weight[0], "seq", axis=1, tiled=True),
        preferred_element_type=jnp.float32,
    ).astype(jnp.bfloat16)
    return mixed.reshape(1, rows, mixed.shape[-1])


def solution(mesh):
    in_specs = (
        P(("dom", "seq"), None),
        P(("dom", "seq"), None),
        P(("dom", "seq"), None),
        P(("dom", "seq"), None),
        P(("dom", "seq"), None),
        P("dom", "seq", None),
        P("dom", None, "seq"),
        P("dom", None),
        P("dom", None),
    )
    out_specs = P("dom", "seq", None)
    return jax.shard_map(
        per_device, mesh=mesh, in_specs=in_specs, out_specs=out_specs, check_vma=False
    )
```

```python
import jax
import jax.numpy as jnp
from jax import lax
from jax.sharding import PartitionSpec as P

SPAN = 256


def per_device(
    tokens_x, gate_z, in_b, in_c, log_decay, domain_ids, out_weight, norm_gain, skip_gain
):
    groups = lax.axis_size("dom")
    shards = lax.axis_size("seq")
    rows = tokens_x.shape[0]
    seg_rows = rows // groups
    width = tokens_x.shape[1]
    nstate = in_b.shape[1]
    heads = skip_gain.shape[-1]
    hsize = width // heads
    order = jnp.argsort(domain_ids.reshape(groups))

    def arrange(value_rows):
        return jnp.take(value_rows.reshape(groups, seg_rows, value_rows.shape[-1]), order, axis=0)

    pad = (-log_decay.shape[1]) % 128
    packed = jnp.concatenate(
        [tokens_x, in_b, in_c, log_decay, jnp.zeros((rows, pad), log_decay.dtype)], axis=1
    )
    packed = lax.all_to_all(arrange(packed), "dom", split_axis=0, concat_axis=0, tiled=True)
    packed = packed.reshape(rows, packed.shape[-1])
    zs = lax.all_to_all(arrange(gate_z), "dom", split_axis=0, concat_axis=0, tiled=True)
    zs = zs.reshape(rows, width)
    xs = packed[:, :width]
    bs = packed[:, width : width + nstate]
    cs = packed[:, width + nstate : width + 2 * nstate]
    ls = packed[:, width + 2 * nstate : width + 2 * nstate + heads]

    local = width // shards
    lheads = heads // shards
    xbc = jnp.concatenate(
        [
            jnp.transpose(xs.reshape(rows, shards, local), (1, 0, 2)),
            jnp.broadcast_to(bs[None], (shards, rows, nstate)),
            jnp.broadcast_to(cs[None], (shards, rows, nstate)),
        ],
        axis=2,
    )
    xbc = lax.all_to_all(xbc, "seq", split_axis=0, concat_axis=0, tiled=True)
    lsh = jnp.transpose(ls.reshape(rows, shards, lheads), (1, 0, 2))
    lsh = lax.all_to_all(lsh, "seq", split_axis=0, concat_axis=0, tiled=True)

    blocks = shards * rows // SPAN
    xc = xbc[:, :, :local].reshape(blocks, SPAN, lheads, hsize)
    bc = xbc[:, :, local : local + nstate].reshape(blocks, SPAN, nstate)
    cc = xbc[:, :, local + nstate :].reshape(blocks, SPAN, nstate)
    cum = jnp.cumsum(lsh.astype(jnp.float32).reshape(blocks, SPAN, lheads), axis=1)
    scores = jnp.einsum("cin,cjn->cij", cc, bc, preferred_element_type=jnp.float32)
    cum_heads = jnp.transpose(cum, (0, 2, 1))
    diff = cum_heads[:, :, :, None] - cum_heads[:, :, None, :]
    positions = jnp.arange(SPAN)
    lower = positions[:, None] >= positions[None, :]
    decay = jnp.where(lower[None, None], jnp.exp(jnp.minimum(diff, 0.0)), 0.0)
    weights = (scores[:, None] * decay).astype(jnp.bfloat16)
    inner = jnp.einsum("chij,cjhp->cihp", weights, xc, preferred_element_type=jnp.float32)
    totals = cum[:, -1, :]
    decayed = (xc.astype(jnp.float32) * jnp.exp(totals[:, None, :] - cum)[..., None]).astype(
        jnp.bfloat16
    )
    block_state = jnp.einsum("cjhp,cjn->chpn", decayed, bc, preferred_element_type=jnp.float32)

    idx = jnp.arange(blocks)
    between = (idx[None, :, None] < idx[None, None, :]) & (idx[None, None, :] < idx[:, None, None])
    gaps = jnp.einsum(
        "kji,ih->hkj", between.astype(jnp.float32), totals, precision=lax.Precision.HIGHEST
    )
    earlier = idx[None, :] < idx[:, None]
    carry = jnp.where(earlier[None], jnp.exp(jnp.minimum(gaps, 0.0)), 0.0)
    before = jnp.einsum("hkj,jhpn->khpn", carry, block_state, precision=lax.Precision.HIGHEST)
    carried = jnp.einsum(
        "cin,chpn->cihp", cc.astype(jnp.float32), before, precision=lax.Precision.HIGHEST
    )
    skip = lax.dynamic_slice_in_dim(skip_gain[0], lax.axis_index("seq") * lheads, lheads)
    ys = (
        inner
        + jnp.exp(cum)[..., None] * carried
        + skip[None, None, :, None] * xc.astype(jnp.float32)
    )

    ys = lax.all_to_all(
        ys.reshape(shards, rows, local).astype(jnp.bfloat16),
        "seq",
        split_axis=0,
        concat_axis=0,
        tiled=True,
    ).astype(jnp.float32)
    ys = jnp.transpose(ys, (1, 0, 2)).reshape(rows, width)
    gated = ys * jax.nn.silu(zs.astype(jnp.float32))
    normed = (
        gated
        * lax.rsqrt(jnp.mean(gated * gated, axis=-1, keepdims=True) + 1e-05)
        * norm_gain[0][None, :]
    ).astype(jnp.bfloat16)
    mixed = jnp.dot(
        normed,
        lax.all_gather(out_weight[0], "seq", axis=1, tiled=True),
        preferred_element_type=jnp.float32,
    ).astype(jnp.bfloat16)
    return mixed.reshape(1, rows, mixed.shape[-1])


def solution(mesh):
    in_specs = (
        P(("dom", "seq"), None),
        P(("dom", "seq"), None),
        P(("dom", "seq"), None),
        P(("dom", "seq"), None),
        P(("dom", "seq"), None),
        P("dom", "seq", None),
        P("dom", None, "seq"),
        P("dom", None),
        P("dom", None),
    )
    out_specs = P("dom", "seq", None)
    return jax.shard_map(
        per_device, mesh=mesh, in_specs=in_specs, out_specs=out_specs, check_vma=False
    )
```

```python
import jax
import jax.numpy as jnp
from jax import lax
from jax.sharding import PartitionSpec as P

SPAN = 256


def per_device(
    tokens_x, gate_z, in_b, in_c, log_decay, domain_ids, out_weight, norm_gain, skip_gain
):
    groups = lax.axis_size("dom")
    shards = lax.axis_size("seq")
    rows = tokens_x.shape[0]
    seg_rows = rows // groups
    width = tokens_x.shape[1]
    nstate = in_b.shape[1]
    heads = skip_gain.shape[-1]
    hsize = width // heads
    order = jnp.argsort(domain_ids.reshape(groups))

    def arrange(value_rows):
        return jnp.take(value_rows.reshape(groups, seg_rows, value_rows.shape[-1]), order, axis=0)

    pad = (-log_decay.shape[1]) % 128
    packed = jnp.concatenate(
        [tokens_x, in_b, in_c, log_decay, jnp.zeros((rows, pad), log_decay.dtype)], axis=1
    )
    packed = lax.all_to_all(arrange(packed), "dom", split_axis=0, concat_axis=0, tiled=True)
    packed = packed.reshape(rows, packed.shape[-1])
    zs = lax.all_to_all(arrange(gate_z), "dom", split_axis=0, concat_axis=0, tiled=True)
    zs = zs.reshape(rows, width)
    xs = packed[:, :width]
    bs = packed[:, width : width + nstate]
    cs = packed[:, width + nstate : width + 2 * nstate]
    ls = packed[:, width + 2 * nstate : width + 2 * nstate + heads]

    local = width // shards
    lheads = heads // shards
    xbc = jnp.concatenate(
        [
            jnp.transpose(xs.reshape(rows, shards, local), (1, 0, 2)),
            jnp.broadcast_to(bs[None], (shards, rows, nstate)),
            jnp.broadcast_to(cs[None], (shards, rows, nstate)),
        ],
        axis=2,
    )
    xbc = lax.all_to_all(xbc, "seq", split_axis=0, concat_axis=0, tiled=True)
    lsh = jnp.transpose(ls.reshape(rows, shards, lheads), (1, 0, 2))
    lsh = lax.all_to_all(lsh, "seq", split_axis=0, concat_axis=0, tiled=True)

    blocks = shards * rows // SPAN
    xc = xbc[:, :, :local].reshape(blocks, SPAN, lheads, hsize)
    bc = xbc[:, :, local : local + nstate].reshape(blocks, SPAN, nstate)
    cc = xbc[:, :, local + nstate :].reshape(blocks, SPAN, nstate)
    cum = jnp.cumsum(lsh.astype(jnp.float32).reshape(blocks, SPAN, lheads), axis=1)
    scores = jnp.einsum("cin,cjn->cij", cc, bc, preferred_element_type=jnp.float32)
    cum_heads = jnp.transpose(cum, (0, 2, 1))
    diff = cum_heads[:, :, :, None] - cum_heads[:, :, None, :]
    positions = jnp.arange(SPAN)
    lower = positions[:, None] >= positions[None, :]
    decay = jnp.where(lower[None, None], jnp.exp(jnp.minimum(diff, 0.0)), 0.0)
    weights = (scores[:, None] * decay).astype(jnp.bfloat16)
    inner = jnp.einsum("chij,cjhp->cihp", weights, xc, preferred_element_type=jnp.float32)
    totals = cum[:, -1, :]
    decayed = (xc.astype(jnp.float32) * jnp.exp(totals[:, None, :] - cum)[..., None]).astype(
        jnp.bfloat16
    )
    block_state = jnp.einsum("cjhp,cjn->chpn", decayed, bc, preferred_element_type=jnp.float32)

    idx = jnp.arange(blocks)
    between = (idx[None, :, None] < idx[None, None, :]) & (idx[None, None, :] < idx[:, None, None])
    gaps = jnp.einsum(
        "kji,ih->hkj", between.astype(jnp.float32), totals, precision=lax.Precision.HIGHEST
    )
    earlier = idx[None, :] < idx[:, None]
    carry = jnp.where(earlier[None], jnp.exp(jnp.minimum(gaps, 0.0)), 0.0)
    before = jnp.einsum("hkj,jhpn->khpn", carry, block_state, precision=lax.Precision.HIGHEST)
    carried = jnp.einsum(
        "cin,chpn->cihp", cc.astype(jnp.float32), before, precision=lax.Precision.HIGHEST
    )
    skip = lax.dynamic_slice_in_dim(skip_gain[0], lax.axis_index("seq") * lheads, lheads)
    ys = (
        inner
        + jnp.exp(cum)[..., None] * carried
        + skip[None, None, :, None] * xc.astype(jnp.float32)
    )

    amax = jnp.max(jnp.abs(ys), axis=-1, keepdims=True)
    scale = amax / 32767.0
    coded = jnp.clip(jnp.round(ys / jnp.where(scale > 0, scale, 1.0)), -32767.0, 32767.0)
    coded = lax.all_to_all(
        coded.astype(jnp.int16).reshape(shards, rows, local),
        "seq",
        split_axis=0,
        concat_axis=0,
        tiled=True,
    )
    scale = lax.all_to_all(
        scale.reshape(shards, rows, lheads), "seq", split_axis=0, concat_axis=0, tiled=True
    )
    ys = coded.reshape(shards, rows, lheads, hsize).astype(jnp.float32) * scale[..., None]
    ys = ys.reshape(shards, rows, local)
    ys = jnp.transpose(ys, (1, 0, 2)).reshape(rows, width)
    gated = ys * jax.nn.silu(zs.astype(jnp.float32))
    normed = (
        gated
        * lax.rsqrt(jnp.mean(gated * gated, axis=-1, keepdims=True) + 1e-05)
        * norm_gain[0][None, :]
    ).astype(jnp.bfloat16)
    mixed = jnp.dot(
        normed,
        lax.all_gather(out_weight[0], "seq", axis=1, tiled=True),
        preferred_element_type=jnp.float32,
    ).astype(jnp.bfloat16)
    return mixed.reshape(1, rows, mixed.shape[-1])


def solution(mesh):
    in_specs = (
        P(("dom", "seq"), None),
        P(("dom", "seq"), None),
        P(("dom", "seq"), None),
        P(("dom", "seq"), None),
        P(("dom", "seq"), None),
        P("dom", "seq", None),
        P("dom", None, "seq"),
        P("dom", None),
        P("dom", None),
    )
    out_specs = P("dom", "seq", None)
    return jax.shard_map(
        per_device, mesh=mesh, in_specs=in_specs, out_specs=out_specs, check_vma=False
    )
```

```python
import jax
import jax.numpy as jnp
import numpy as np
from jax import lax
from jax.sharding import Mesh
from jax.sharding import PartitionSpec as P

SPAN = 256
SEQ = ("sx", "sz")


def code16(values, axis_name):
    amax = jnp.max(jnp.abs(values), axis=-1, keepdims=True)
    scale = amax / 32767.0
    coded = jnp.clip(jnp.round(values / jnp.where(scale > 0, scale, 1.0)), -32767.0, 32767.0)
    lead = values.shape[:2]
    coded = lax.all_to_all(
        coded.astype(jnp.int16).reshape(*lead, -1), axis_name, split_axis=0, concat_axis=0, tiled=True
    )
    scale = lax.all_to_all(
        scale.reshape(*lead, -1), axis_name, split_axis=0, concat_axis=0, tiled=True
    )
    return coded.reshape(values.shape).astype(jnp.float32) * scale[..., None]


def per_device(
    tokens_x, gate_z, in_b, in_c, log_decay, domain_ids, out_weight, norm_gain, skip_gain
):
    groups = lax.axis_size("dom")
    nx = lax.axis_size("sx")
    nz = lax.axis_size("sz")
    rows = tokens_x.shape[0]
    seg_rows = rows // groups
    width = tokens_x.shape[1]
    nstate = in_b.shape[1]
    heads = skip_gain.shape[-1]
    hsize = width // heads
    order = jnp.argsort(domain_ids.reshape(groups))

    def arrange(value_rows):
        return jnp.take(value_rows.reshape(groups, seg_rows, value_rows.shape[-1]), order, axis=0)

    pad = (-log_decay.shape[1]) % 128
    packed = jnp.concatenate(
        [tokens_x, in_b, in_c, log_decay, jnp.zeros((rows, pad), log_decay.dtype)], axis=1
    )
    packed = lax.all_to_all(arrange(packed), "dom", split_axis=0, concat_axis=0, tiled=True)
    packed = packed.reshape(rows, packed.shape[-1])
    zs = lax.all_to_all(arrange(gate_z), "dom", split_axis=0, concat_axis=0, tiled=True)
    zs = zs.reshape(rows, width)
    xs = packed[:, :width]
    bs = packed[:, width : width + nstate]
    cs = packed[:, width + nstate : width + 2 * nstate]
    ls = packed[:, width + 2 * nstate : width + 2 * nstate + heads]

    local = width // nz
    lheads = heads // nz
    xbc = jnp.concatenate(
        [
            jnp.transpose(xs.reshape(rows, nz, local), (1, 0, 2)),
            jnp.broadcast_to(bs[None], (nz, rows, nstate)),
            jnp.broadcast_to(cs[None], (nz, rows, nstate)),
        ],
        axis=2,
    )
    xbc = lax.all_to_all(xbc, "sz", split_axis=0, concat_axis=0, tiled=True)
    lsh = jnp.transpose(ls.reshape(rows, nz, lheads), (1, 0, 2))
    lsh = lax.all_to_all(lsh, "sz", split_axis=0, concat_axis=0, tiled=True)

    blocks = nz * rows // SPAN
    xc = xbc[:, :, :local].reshape(blocks, SPAN, lheads, hsize)
    bc = xbc[:, :, local : local + nstate].reshape(blocks, SPAN, nstate)
    cc = xbc[:, :, local + nstate :].reshape(blocks, SPAN, nstate)
    cum = jnp.cumsum(lsh.astype(jnp.float32).reshape(blocks, SPAN, lheads), axis=1)
    scores = jnp.einsum("cin,cjn->cij", cc, bc, preferred_element_type=jnp.float32)
    cum_heads = jnp.transpose(cum, (0, 2, 1))
    diff = cum_heads[:, :, :, None] - cum_heads[:, :, None, :]
    positions = jnp.arange(SPAN)
    lower = positions[:, None] >= positions[None, :]
    decay = jnp.where(lower[None, None], jnp.exp(jnp.minimum(diff, 0.0)), 0.0)
    weights = (scores[:, None] * decay).astype(jnp.bfloat16)
    inner = jnp.einsum("chij,cjhp->cihp", weights, xc, preferred_element_type=jnp.float32)
    totals = cum[:, -1, :]
    decayed = (xc.astype(jnp.float32) * jnp.exp(totals[:, None, :] - cum)[..., None]).astype(
        jnp.bfloat16
    )
    block_state = jnp.einsum("cjhp,cjn->chpn", decayed, bc, preferred_element_type=jnp.float32)

    kdx = jnp.arange(blocks + 1)
    jdx = jnp.arange(blocks)
    between = (jdx[None, :, None] < jdx[None, None, :]) & (jdx[None, None, :] < kdx[:, None, None])
    gaps = jnp.einsum(
        "kji,ih->hkj", between.astype(jnp.float32), totals, precision=lax.Precision.HIGHEST
    )
    earlier = jdx[None, :] < kdx[:, None]
    carry = jnp.where(earlier[None], jnp.exp(jnp.minimum(gaps, 0.0)), 0.0)
    before = jnp.einsum("hkj,jhpn->khpn", carry, block_state, precision=lax.Precision.HIGHEST)
    local_end = before[blocks]
    before = before[:blocks]
    shard_total = jnp.sum(totals, axis=0)

    slab = jnp.pad(shard_total, (0, hsize - lheads))
    ends = jnp.concatenate(
        [local_end, jnp.broadcast_to(slab[None, :, None], (1, hsize, nstate))], axis=0
    )
    ends = lax.all_to_all(
        jnp.broadcast_to(ends[None], (nx,) + ends.shape), "sx", split_axis=0, concat_axis=0, tiled=True
    )
    end_states = ends[:, :lheads]
    end_totals = ends[:, lheads, :lheads, 0]
    me = lax.axis_index("sx")
    xdx = jnp.arange(nx)
    inside = ((xdx[:, None] < xdx[None, :]) & (xdx[None, :] < me)).astype(jnp.float32)
    gap_x = jnp.einsum("ji,ih->jh", inside, end_totals, precision=lax.Precision.HIGHEST)
    weight_x = jnp.where((xdx < me)[:, None], jnp.exp(jnp.minimum(gap_x, 0.0)), 0.0)
    incoming = jnp.einsum("jh,jhpn->hpn", weight_x, end_states, precision=lax.Precision.HIGHEST)
    prefix = jnp.cumsum(totals, axis=0) - totals
    before = before + jnp.exp(prefix)[:, :, None, None] * incoming[None]

    carried = jnp.einsum(
        "cin,chpn->cihp", cc.astype(jnp.float32), before, precision=lax.Precision.HIGHEST
    )
    skip = lax.dynamic_slice_in_dim(skip_gain[0], lax.axis_index("sz") * lheads, lheads)
    ys = (
        inner
        + jnp.exp(cum)[..., None] * carried
        + skip[None, None, :, None] * xc.astype(jnp.float32)
    )

    ys = code16(ys, "sz").reshape(nz, rows, local)
    ys = jnp.transpose(ys, (1, 0, 2)).reshape(rows, width)
    gated = ys * jax.nn.silu(zs.astype(jnp.float32))
    normed = (
        gated
        * lax.rsqrt(jnp.mean(gated * gated, axis=-1, keepdims=True) + 1e-05)
        * norm_gain[0][None, :]
    ).astype(jnp.bfloat16)
    mixed = jnp.dot(
        normed,
        lax.all_gather(out_weight[0], SEQ, axis=1, tiled=True),
        preferred_element_type=jnp.float32,
    ).astype(jnp.bfloat16)
    return mixed.reshape(1, rows, mixed.shape[-1])


def solution(mesh):
    shards = mesh.shape["seq"]
    inner = 4 if shards % 4 == 0 else shards
    split = Mesh(
        np.asarray(mesh.devices).reshape(mesh.shape["dom"], shards // inner, inner),
        ("dom",) + SEQ,
    )
    rows = P(("dom",) + SEQ, None)
    in_specs = (
        rows,
        rows,
        rows,
        rows,
        rows,
        P("dom", SEQ, None),
        P("dom", None, SEQ),
        P("dom", None),
        P("dom", None),
    )
    out_specs = P("dom", SEQ, None)
    return jax.shard_map(
        per_device, mesh=split, in_specs=in_specs, out_specs=out_specs, check_vma=False
    )
```

```python
import jax
import jax.numpy as jnp
import numpy as np
from jax import lax
from jax.sharding import Mesh
from jax.sharding import PartitionSpec as P

SPAN = 256
SEQ = ("sx", "sz")


def code16(values, axis_name):
    amax = jnp.max(jnp.abs(values), axis=-1, keepdims=True)
    scale = amax / 32767.0
    coded = jnp.clip(jnp.round(values / jnp.where(scale > 0, scale, 1.0)), -32767.0, 32767.0)
    lead = values.shape[:2]
    coded = lax.all_to_all(
        coded.astype(jnp.int16).reshape(*lead, -1), axis_name, split_axis=0, concat_axis=0, tiled=True
    )
    scale = lax.all_to_all(
        scale.reshape(*lead, -1), axis_name, split_axis=0, concat_axis=0, tiled=True
    )
    return coded.reshape(values.shape).astype(jnp.float32) * scale[..., None]


def per_device(
    tokens_x, gate_z, in_b, in_c, log_decay, domain_ids, out_weight, norm_gain, skip_gain
):
    groups = lax.axis_size("dom")
    nx = lax.axis_size("sx")
    nz = lax.axis_size("sz")
    rows = tokens_x.shape[0]
    seg_rows = rows // groups
    width = tokens_x.shape[1]
    nstate = in_b.shape[1]
    heads = skip_gain.shape[-1]
    hsize = width // heads
    order = jnp.argsort(domain_ids.reshape(groups))

    def arrange(value_rows):
        return jnp.take(value_rows.reshape(groups, seg_rows, value_rows.shape[-1]), order, axis=0)

    pad = (-log_decay.shape[1]) % 128
    packed = jnp.concatenate(
        [tokens_x, in_b, in_c, log_decay, jnp.zeros((rows, pad), log_decay.dtype)], axis=1
    )
    packed = lax.all_to_all(arrange(packed), "dom", split_axis=0, concat_axis=0, tiled=True)
    packed = packed.reshape(rows, packed.shape[-1])
    zs = lax.all_to_all(arrange(gate_z), "dom", split_axis=0, concat_axis=0, tiled=True)
    zs = zs.reshape(rows, width)
    xs = packed[:, :width]
    bs = packed[:, width : width + nstate]
    cs = packed[:, width + nstate : width + 2 * nstate]
    ls = packed[:, width + 2 * nstate : width + 2 * nstate + heads]

    local = width // nz
    lheads = heads // nz
    xbc = jnp.concatenate(
        [
            jnp.transpose(xs.reshape(rows, nz, local), (1, 0, 2)),
            jnp.broadcast_to(bs[None], (nz, rows, nstate)),
            jnp.broadcast_to(cs[None], (nz, rows, nstate)),
        ],
        axis=2,
    )
    xbc = lax.all_to_all(xbc, "sz", split_axis=0, concat_axis=0, tiled=True)
    lsh = jnp.transpose(ls.reshape(rows, nz, lheads), (1, 0, 2))
    lsh = lax.all_to_all(lsh, "sz", split_axis=0, concat_axis=0, tiled=True)

    blocks = nz * rows // SPAN
    xc = xbc[:, :, :local].reshape(blocks, SPAN, lheads, hsize)
    bc = xbc[:, :, local : local + nstate].reshape(blocks, SPAN, nstate)
    cc = xbc[:, :, local + nstate :].reshape(blocks, SPAN, nstate)
    cum = jnp.cumsum(lsh.astype(jnp.float32).reshape(blocks, SPAN, lheads), axis=1)
    scores = jnp.einsum("cin,cjn->cij", cc, bc, preferred_element_type=jnp.float32)
    cum_heads = jnp.transpose(cum, (0, 2, 1))
    diff = cum_heads[:, :, :, None] - cum_heads[:, :, None, :]
    positions = jnp.arange(SPAN)
    lower = positions[:, None] >= positions[None, :]
    decay = jnp.where(lower[None, None], jnp.exp(jnp.minimum(diff, 0.0)), 0.0)
    weights = (scores[:, None] * decay).astype(jnp.bfloat16)
    inner = jnp.einsum("chij,cjhp->cihp", weights, xc, preferred_element_type=jnp.float32)
    totals = cum[:, -1, :]
    decayed = (xc.astype(jnp.float32) * jnp.exp(totals[:, None, :] - cum)[..., None]).astype(
        jnp.bfloat16
    )
    block_state = jnp.einsum("cjhp,cjn->chpn", decayed, bc, preferred_element_type=jnp.float32)

    kdx = jnp.arange(blocks + 1)
    jdx = jnp.arange(blocks)
    between = (jdx[None, :, None] < jdx[None, None, :]) & (jdx[None, None, :] < kdx[:, None, None])
    gaps = jnp.einsum(
        "kji,ih->hkj", between.astype(jnp.float32), totals, precision=lax.Precision.HIGHEST
    )
    earlier = jdx[None, :] < kdx[:, None]
    carry = jnp.where(earlier[None], jnp.exp(jnp.minimum(gaps, 0.0)), 0.0)
    before = jnp.einsum("hkj,jhpn->khpn", carry, block_state, precision=lax.Precision.HIGHEST)
    local_end = before[blocks]
    before = before[:blocks]
    shard_total = jnp.sum(totals, axis=0)

    slab = jnp.pad(shard_total, (0, hsize - lheads))
    ends = jnp.concatenate(
        [local_end, jnp.broadcast_to(slab[None, :, None], (1, hsize, nstate))], axis=0
    )
    got = [
        lax.ppermute(ends, "sx", [(i, i + d) for i in range(nx - d)]) for d in range(1, nx)
    ]
    incoming = jnp.zeros_like(local_end)
    gap = jnp.zeros((lheads,), jnp.float32)
    for piece in got:
        incoming = incoming + jnp.exp(gap)[:, None, None] * piece[:lheads]
        gap = gap + piece[lheads, :lheads, 0]
    prefix = jnp.cumsum(totals, axis=0) - totals
    before = before + jnp.exp(prefix)[:, :, None, None] * incoming[None]

    carried = jnp.einsum(
        "cin,chpn->cihp", cc.astype(jnp.float32), before, precision=lax.Precision.HIGHEST
    )
    skip = lax.dynamic_slice_in_dim(skip_gain[0], lax.axis_index("sz") * lheads, lheads)
    ys = (
        inner
        + jnp.exp(cum)[..., None] * carried
        + skip[None, None, :, None] * xc.astype(jnp.float32)
    )

    ys = code16(ys, "sz").reshape(nz, rows, local)
    ys = jnp.transpose(ys, (1, 0, 2)).reshape(rows, width)
    gated = ys * jax.nn.silu(zs.astype(jnp.float32))
    normed = (
        gated
        * lax.rsqrt(jnp.mean(gated * gated, axis=-1, keepdims=True) + 1e-05)
        * norm_gain[0][None, :]
    ).astype(jnp.bfloat16)
    mixed = jnp.dot(
        normed,
        lax.all_gather(out_weight[0], SEQ, axis=1, tiled=True),
        preferred_element_type=jnp.float32,
    ).astype(jnp.bfloat16)
    return mixed.reshape(1, rows, mixed.shape[-1])


def solution(mesh):
    shards = mesh.shape["seq"]
    inner = 4 if shards % 4 == 0 else shards
    split = Mesh(
        np.asarray(mesh.devices).reshape(mesh.shape["dom"], shards // inner, inner),
        ("dom",) + SEQ,
    )
    rows = P(("dom",) + SEQ, None)
    in_specs = (
        rows,
        rows,
        rows,
        rows,
        rows,
        P("dom", SEQ, None),
        P("dom", None, SEQ),
        P("dom", None),
        P("dom", None),
    )
    out_specs = P("dom", SEQ, None)
    return jax.shard_map(
        per_device, mesh=split, in_specs=in_specs, out_specs=out_specs, check_vma=False
    )
```

```python
import jax
import jax.numpy as jnp
import numpy as np
from jax import lax
from jax.sharding import Mesh
from jax.sharding import PartitionSpec as P

SPAN = 256
SEQ = ("sx", "sz")


def code16(values, axis_name):
    amax = jnp.max(jnp.abs(values), axis=-1, keepdims=True)
    scale = amax / 32767.0
    coded = jnp.clip(jnp.round(values / jnp.where(scale > 0, scale, 1.0)), -32767.0, 32767.0)
    lead = values.shape[:2]
    coded = lax.all_to_all(
        coded.astype(jnp.int16).reshape(*lead, -1), axis_name, split_axis=0, concat_axis=0, tiled=True
    )
    scale = lax.all_to_all(
        scale.reshape(*lead, -1), axis_name, split_axis=0, concat_axis=0, tiled=True
    )
    return coded.reshape(values.shape).astype(jnp.float32) * scale[..., None]


def per_device(
    tokens_x, gate_z, in_b, in_c, log_decay, domain_ids, out_weight, norm_gain, skip_gain
):
    groups = lax.axis_size("dom")
    nx = lax.axis_size("sx")
    nz = lax.axis_size("sz")
    rows = tokens_x.shape[0]
    seg_rows = rows // groups
    width = tokens_x.shape[1]
    nstate = in_b.shape[1]
    heads = skip_gain.shape[-1]
    hsize = width // heads
    order = jnp.argsort(domain_ids.reshape(groups))

    def arrange(value_rows):
        return jnp.take(value_rows.reshape(groups, seg_rows, value_rows.shape[-1]), order, axis=0)

    pad = (-log_decay.shape[1]) % 128
    packed = jnp.concatenate(
        [tokens_x, in_b, in_c, log_decay, jnp.zeros((rows, pad), log_decay.dtype)], axis=1
    )
    packed = lax.all_to_all(arrange(packed), "dom", split_axis=0, concat_axis=0, tiled=True)
    packed = packed.reshape(rows, packed.shape[-1])
    zs = lax.all_to_all(arrange(gate_z), "dom", split_axis=0, concat_axis=0, tiled=True)
    zs = zs.reshape(rows, width)
    xs = packed[:, :width]
    bs = packed[:, width : width + nstate]
    cs = packed[:, width + nstate : width + 2 * nstate]
    ls = packed[:, width + 2 * nstate : width + 2 * nstate + heads]

    local = width // nz
    lheads = heads // nz
    xbc = jnp.concatenate(
        [
            jnp.transpose(xs.reshape(rows, nz, local), (1, 0, 2)),
            jnp.broadcast_to(bs[None], (nz, rows, nstate)),
            jnp.broadcast_to(cs[None], (nz, rows, nstate)),
        ],
        axis=2,
    )
    xbc = lax.all_to_all(xbc, "sz", split_axis=0, concat_axis=0, tiled=True)
    lsh = jnp.transpose(ls.reshape(rows, nz, lheads), (1, 0, 2))
    lsh = lax.all_to_all(lsh, "sz", split_axis=0, concat_axis=0, tiled=True)

    blocks = nz * rows // SPAN
    xc = xbc[:, :, :local].reshape(blocks, SPAN, lheads, hsize)
    bc = xbc[:, :, local : local + nstate].reshape(blocks, SPAN, nstate)
    cc = xbc[:, :, local + nstate :].reshape(blocks, SPAN, nstate)
    cum = jnp.cumsum(lsh.astype(jnp.float32).reshape(blocks, SPAN, lheads), axis=1)
    scores = jnp.einsum("cin,cjn->cij", cc, bc, preferred_element_type=jnp.float32)
    cum_heads = jnp.transpose(cum, (0, 2, 1))
    diff = cum_heads[:, :, :, None] - cum_heads[:, :, None, :]
    positions = jnp.arange(SPAN)
    lower = positions[:, None] >= positions[None, :]
    decay = jnp.where(lower[None, None], jnp.exp(jnp.minimum(diff, 0.0)), 0.0)
    weights = (scores[:, None] * decay).astype(jnp.bfloat16)
    inner = jnp.einsum("chij,cjhp->cihp", weights, xc, preferred_element_type=jnp.float32)
    totals = cum[:, -1, :]
    decayed = (xc.astype(jnp.float32) * jnp.exp(totals[:, None, :] - cum)[..., None]).astype(
        jnp.bfloat16
    )
    block_state = jnp.einsum("cjhp,cjn->chpn", decayed, bc, preferred_element_type=jnp.float32)

    kdx = jnp.arange(blocks + 1)
    jdx = jnp.arange(blocks)
    between = (jdx[None, :, None] < jdx[None, None, :]) & (jdx[None, None, :] < kdx[:, None, None])
    gaps = jnp.einsum(
        "kji,ih->hkj", between.astype(jnp.float32), totals, precision=lax.Precision.HIGHEST
    )
    earlier = jdx[None, :] < kdx[:, None]
    carry = jnp.where(earlier[None], jnp.exp(jnp.minimum(gaps, 0.0)), 0.0)
    before = jnp.einsum("hkj,jhpn->khpn", carry, block_state, precision=lax.Precision.HIGHEST)
    local_end = before[blocks]
    before = before[:blocks]
    shard_total = jnp.sum(totals, axis=0)

    amax = jnp.max(jnp.abs(local_end), axis=-1, keepdims=True)
    scale = amax / 32767.0
    coded = jnp.clip(
        jnp.round(local_end / jnp.where(scale > 0, scale, 1.0)), -32767.0, 32767.0
    ).astype(jnp.int16)
    lanes = 128
    side = jnp.concatenate(
        [scale.reshape(-1), shard_total, jnp.zeros((lanes - lheads,), jnp.float32)]
    ).reshape(-1, lanes)
    incoming = jnp.zeros_like(local_end)
    gap = jnp.zeros((lheads,), jnp.float32)
    for d in range(1, nx):
        route = [(i, i + d) for i in range(nx - d)]
        piece = lax.ppermute(coded, "sx", route).astype(jnp.float32)
        got = lax.ppermute(side, "sx", route).reshape(-1)
        piece = piece * got[: lheads * hsize].reshape(lheads, hsize, 1)
        incoming = incoming + jnp.exp(gap)[:, None, None] * piece
        gap = gap + got[lheads * hsize : lheads * hsize + lheads]
    prefix = jnp.cumsum(totals, axis=0) - totals
    before = before + jnp.exp(prefix)[:, :, None, None] * incoming[None]

    carried = jnp.einsum(
        "cin,chpn->cihp", cc.astype(jnp.float32), before, precision=lax.Precision.HIGHEST
    )
    skip = lax.dynamic_slice_in_dim(skip_gain[0], lax.axis_index("sz") * lheads, lheads)
    ys = (
        inner
        + jnp.exp(cum)[..., None] * carried
        + skip[None, None, :, None] * xc.astype(jnp.float32)
    )

    ys = code16(ys, "sz").reshape(nz, rows, local)
    ys = jnp.transpose(ys, (1, 0, 2)).reshape(rows, width)
    gated = ys * jax.nn.silu(zs.astype(jnp.float32))
    normed = (
        gated
        * lax.rsqrt(jnp.mean(gated * gated, axis=-1, keepdims=True) + 1e-05)
        * norm_gain[0][None, :]
    ).astype(jnp.bfloat16)
    mixed = jnp.dot(
        normed,
        lax.all_gather(out_weight[0], SEQ, axis=1, tiled=True),
        preferred_element_type=jnp.float32,
    ).astype(jnp.bfloat16)
    return mixed.reshape(1, rows, mixed.shape[-1])


def solution(mesh):
    shards = mesh.shape["seq"]
    inner = 4 if shards % 4 == 0 else shards
    split = Mesh(
        np.asarray(mesh.devices).reshape(mesh.shape["dom"], shards // inner, inner),
        ("dom",) + SEQ,
    )
    rows = P(("dom",) + SEQ, None)
    in_specs = (
        rows,
        rows,
        rows,
        rows,
        rows,
        P("dom", SEQ, None),
        P("dom", None, SEQ),
        P("dom", None),
        P("dom", None),
    )
    out_specs = P("dom", SEQ, None)
    return jax.shard_map(
        per_device, mesh=split, in_specs=in_specs, out_specs=out_specs, check_vma=False
    )
```

```python
import jax
import jax.numpy as jnp
import numpy as np
from jax import lax
from jax.experimental import pallas as pl
from jax.experimental.pallas import tpu as pltpu
from jax.sharding import Mesh
from jax.sharding import PartitionSpec as P

SPAN = 256
SEQ = ("sx", "sz")


def code16(values, axis_name):
    amax = jnp.max(jnp.abs(values), axis=-1, keepdims=True)
    scale = amax / 32767.0
    coded = jnp.clip(jnp.round(values / jnp.where(scale > 0, scale, 1.0)), -32767.0, 32767.0)
    lead = values.shape[:2]
    coded = lax.all_to_all(
        coded.astype(jnp.int16).reshape(*lead, -1), axis_name, split_axis=0, concat_axis=0, tiled=True
    )
    scale = lax.all_to_all(
        scale.reshape(*lead, -1), axis_name, split_axis=0, concat_axis=0, tiled=True
    )
    return coded.reshape(values.shape).astype(jnp.float32) * scale[..., None]


def project_kernel(a_ref, w_ref, o_ref):
    o_ref[...] = jnp.dot(a_ref[...], w_ref[...], preferred_element_type=jnp.float32).astype(
        o_ref.dtype
    )


def project(normed, weight, tile=512):
    rows, depth = normed.shape
    cols = weight.shape[1]
    return pl.pallas_call(
        project_kernel,
        grid=(cols // tile,),
        in_specs=[
            pl.BlockSpec((rows, depth), lambda j: (0, 0)),
            pl.BlockSpec((depth, tile), lambda j: (0, j)),
        ],
        out_specs=pl.BlockSpec((rows, tile), lambda j: (0, j)),
        out_shape=jax.ShapeDtypeStruct((rows, cols), jnp.bfloat16),
        compiler_params=pltpu.CompilerParams(vmem_limit_bytes=48 * 1024 * 1024),
    )(normed, weight)


def per_device(
    tokens_x, gate_z, in_b, in_c, log_decay, domain_ids, out_weight, norm_gain, skip_gain
):
    groups = lax.axis_size("dom")
    nx = lax.axis_size("sx")
    nz = lax.axis_size("sz")
    rows = tokens_x.shape[0]
    seg_rows = rows // groups
    width = tokens_x.shape[1]
    nstate = in_b.shape[1]
    heads = skip_gain.shape[-1]
    hsize = width // heads
    order = jnp.argsort(domain_ids.reshape(groups))

    def arrange(value_rows):
        return jnp.take(value_rows.reshape(groups, seg_rows, value_rows.shape[-1]), order, axis=0)

    pad = (-log_decay.shape[1]) % 128
    packed = jnp.concatenate(
        [tokens_x, in_b, in_c, log_decay, jnp.zeros((rows, pad), log_decay.dtype)], axis=1
    )
    packed = lax.all_to_all(arrange(packed), "dom", split_axis=0, concat_axis=0, tiled=True)
    packed = packed.reshape(rows, packed.shape[-1])
    zs = lax.all_to_all(arrange(gate_z), "dom", split_axis=0, concat_axis=0, tiled=True)
    zs = zs.reshape(rows, width)
    xs = packed[:, :width]
    bs = packed[:, width : width + nstate]
    cs = packed[:, width + nstate : width + 2 * nstate]
    ls = packed[:, width + 2 * nstate : width + 2 * nstate + heads]

    local = width // nz
    lheads = heads // nz
    xbc = jnp.concatenate(
        [
            jnp.transpose(xs.reshape(rows, nz, local), (1, 0, 2)),
            jnp.broadcast_to(bs[None], (nz, rows, nstate)),
            jnp.broadcast_to(cs[None], (nz, rows, nstate)),
        ],
        axis=2,
    )
    xbc = lax.all_to_all(xbc, "sz", split_axis=0, concat_axis=0, tiled=True)
    lsh = jnp.transpose(ls.reshape(rows, nz, lheads), (1, 0, 2))
    lsh = lax.all_to_all(lsh, "sz", split_axis=0, concat_axis=0, tiled=True)

    blocks = nz * rows // SPAN
    xc = xbc[:, :, :local].reshape(blocks, SPAN, lheads, hsize)
    bc = xbc[:, :, local : local + nstate].reshape(blocks, SPAN, nstate)
    cc = xbc[:, :, local + nstate :].reshape(blocks, SPAN, nstate)
    cum = jnp.cumsum(lsh.astype(jnp.float32).reshape(blocks, SPAN, lheads), axis=1)
    scores = jnp.einsum("cin,cjn->cij", cc, bc, preferred_element_type=jnp.float32)
    cum_heads = jnp.transpose(cum, (0, 2, 1))
    diff = cum_heads[:, :, :, None] - cum_heads[:, :, None, :]
    positions = jnp.arange(SPAN)
    lower = positions[:, None] >= positions[None, :]
    decay = jnp.where(lower[None, None], jnp.exp(jnp.minimum(diff, 0.0)), 0.0)
    weights = (scores[:, None] * decay).astype(jnp.bfloat16)
    inner = jnp.einsum("chij,cjhp->cihp", weights, xc, preferred_element_type=jnp.float32)
    totals = cum[:, -1, :]
    decayed = (xc.astype(jnp.float32) * jnp.exp(totals[:, None, :] - cum)[..., None]).astype(
        jnp.bfloat16
    )
    block_state = jnp.einsum("cjhp,cjn->chpn", decayed, bc, preferred_element_type=jnp.float32)

    kdx = jnp.arange(blocks + 1)
    jdx = jnp.arange(blocks)
    between = (jdx[None, :, None] < jdx[None, None, :]) & (jdx[None, None, :] < kdx[:, None, None])
    gaps = jnp.einsum(
        "kji,ih->hkj", between.astype(jnp.float32), totals, precision=lax.Precision.HIGHEST
    )
    earlier = jdx[None, :] < kdx[:, None]
    carry = jnp.where(earlier[None], jnp.exp(jnp.minimum(gaps, 0.0)), 0.0)
    before = jnp.einsum("hkj,jhpn->khpn", carry, block_state, precision=lax.Precision.HIGHEST)
    local_end = before[blocks]
    before = before[:blocks]
    shard_total = jnp.sum(totals, axis=0)

    amax = jnp.max(jnp.abs(local_end), axis=-1, keepdims=True)
    scale = amax / 32767.0
    coded = jnp.clip(
        jnp.round(local_end / jnp.where(scale > 0, scale, 1.0)), -32767.0, 32767.0
    ).astype(jnp.int16)
    lanes = 128
    side = jnp.concatenate(
        [scale.reshape(-1), shard_total, jnp.zeros((lanes - lheads,), jnp.float32)]
    ).reshape(-1, lanes)
    incoming = jnp.zeros_like(local_end)
    gap = jnp.zeros((lheads,), jnp.float32)
    for d in range(1, nx):
        route = [(i, i + d) for i in range(nx - d)]
        piece = lax.ppermute(coded, "sx", route).astype(jnp.float32)
        got = lax.ppermute(side, "sx", route).reshape(-1)
        piece = piece * got[: lheads * hsize].reshape(lheads, hsize, 1)
        incoming = incoming + jnp.exp(gap)[:, None, None] * piece
        gap = gap + got[lheads * hsize : lheads * hsize + lheads]
    prefix = jnp.cumsum(totals, axis=0) - totals
    before = before + jnp.exp(prefix)[:, :, None, None] * incoming[None]

    carried = jnp.einsum(
        "cin,chpn->cihp", cc.astype(jnp.float32), before, precision=lax.Precision.HIGHEST
    )
    skip = lax.dynamic_slice_in_dim(skip_gain[0], lax.axis_index("sz") * lheads, lheads)
    ys = (
        inner
        + jnp.exp(cum)[..., None] * carried
        + skip[None, None, :, None] * xc.astype(jnp.float32)
    )

    ys = code16(ys, "sz").reshape(nz, rows, local)
    ys = jnp.transpose(ys, (1, 0, 2)).reshape(rows, width)
    gated = ys * jax.nn.silu(zs.astype(jnp.float32))
    normed = (
        gated
        * lax.rsqrt(jnp.mean(gated * gated, axis=-1, keepdims=True) + 1e-05)
        * norm_gain[0][None, :]
    ).astype(jnp.bfloat16)
    mixed = project(normed, lax.all_gather(out_weight[0], SEQ, axis=1, tiled=True))
    return mixed.reshape(1, rows, mixed.shape[-1])


def solution(mesh):
    shards = mesh.shape["seq"]
    inner = 4 if shards % 4 == 0 else shards
    split = Mesh(
        np.asarray(mesh.devices).reshape(mesh.shape["dom"], shards // inner, inner),
        ("dom",) + SEQ,
    )
    rows = P(("dom",) + SEQ, None)
    in_specs = (
        rows,
        rows,
        rows,
        rows,
        rows,
        P("dom", SEQ, None),
        P("dom", None, SEQ),
        P("dom", None),
        P("dom", None),
    )
    out_specs = P("dom", SEQ, None)
    return jax.shard_map(
        per_device, mesh=split, in_specs=in_specs, out_specs=out_specs, check_vma=False
    )
```

```python
import jax
import jax.numpy as jnp
import numpy as np
from jax import lax
from jax.sharding import Mesh
from jax.sharding import PartitionSpec as P

SPAN = 256
SEQ = ("sx", "sz")


def code16(values, axis_name):
    amax = jnp.max(jnp.abs(values), axis=-1, keepdims=True)
    scale = amax / 32767.0
    coded = jnp.clip(jnp.round(values / jnp.where(scale > 0, scale, 1.0)), -32767.0, 32767.0)
    lead = values.shape[:2]
    coded = lax.all_to_all(
        coded.astype(jnp.int16).reshape(*lead, -1), axis_name, split_axis=0, concat_axis=0, tiled=True
    )
    scale = lax.all_to_all(
        scale.reshape(*lead, -1), axis_name, split_axis=0, concat_axis=0, tiled=True
    )
    return coded.reshape(values.shape).astype(jnp.float32) * scale[..., None]


def per_device(
    tokens_x, gate_z, in_b, in_c, log_decay, domain_ids, out_weight, norm_gain, skip_gain
):
    groups = lax.axis_size("dom")
    nx = lax.axis_size("sx")
    nz = lax.axis_size("sz")
    rows = tokens_x.shape[0]
    seg_rows = rows // groups
    width = tokens_x.shape[1]
    nstate = in_b.shape[1]
    heads = skip_gain.shape[-1]
    hsize = width // heads
    order = jnp.argsort(domain_ids.reshape(groups))

    def arrange(value_rows):
        return jnp.take(value_rows.reshape(groups, seg_rows, value_rows.shape[-1]), order, axis=0)

    local = width // nz
    lheads = heads // nz
    lanes = 128
    xpart = jnp.transpose(arrange(tokens_x).reshape(groups, seg_rows, nz, local), (0, 2, 1, 3))
    lpart = jnp.transpose(arrange(log_decay).reshape(groups, seg_rows, nz, lheads), (0, 2, 1, 3))
    lpart = jnp.pad(lpart, ((0, 0), (0, 0), (0, 0), (0, lanes - lheads)))
    side = jnp.broadcast_to(
        arrange(jnp.concatenate([in_b, in_c], axis=1))[:, None], (groups, nz, seg_rows, 2 * nstate)
    )
    routed = jnp.concatenate([xpart, side, lpart], axis=3)
    routed = routed.reshape(groups * nz, seg_rows, routed.shape[-1])
    routed = lax.all_to_all(routed, ("dom", "sz"), split_axis=0, concat_axis=0, tiled=True)
    routed = jnp.transpose(routed.reshape(groups, nz, seg_rows, routed.shape[-1]), (1, 0, 2, 3))
    routed = routed.reshape(nz * rows, routed.shape[-1])
    zs = lax.all_to_all(arrange(gate_z), "dom", split_axis=0, concat_axis=0, tiled=True)
    zs = zs.reshape(rows, width)

    blocks = nz * rows // SPAN
    xc = routed[:, :local].reshape(blocks, SPAN, lheads, hsize)
    bc = routed[:, local : local + nstate].reshape(blocks, SPAN, nstate)
    cc = routed[:, local + nstate : local + 2 * nstate].reshape(blocks, SPAN, nstate)
    lsh = routed[:, local + 2 * nstate : local + 2 * nstate + lheads]
    cum = jnp.cumsum(lsh.astype(jnp.float32).reshape(blocks, SPAN, lheads), axis=1)
    scores = jnp.einsum("cin,cjn->cij", cc, bc, preferred_element_type=jnp.float32)
    cum_heads = jnp.transpose(cum, (0, 2, 1))
    diff = cum_heads[:, :, :, None] - cum_heads[:, :, None, :]
    positions = jnp.arange(SPAN)
    lower = positions[:, None] >= positions[None, :]
    decay = jnp.where(lower[None, None], jnp.exp(jnp.minimum(diff, 0.0)), 0.0)
    weights = (scores[:, None] * decay).astype(jnp.bfloat16)
    inner = jnp.einsum("chij,cjhp->cihp", weights, xc, preferred_element_type=jnp.float32)
    totals = cum[:, -1, :]
    decayed = (xc.astype(jnp.float32) * jnp.exp(totals[:, None, :] - cum)[..., None]).astype(
        jnp.bfloat16
    )
    block_state = jnp.einsum("cjhp,cjn->chpn", decayed, bc, preferred_element_type=jnp.float32)

    kdx = jnp.arange(blocks + 1)
    jdx = jnp.arange(blocks)
    between = (jdx[None, :, None] < jdx[None, None, :]) & (jdx[None, None, :] < kdx[:, None, None])
    gaps = jnp.einsum(
        "kji,ih->hkj", between.astype(jnp.float32), totals, precision=lax.Precision.HIGHEST
    )
    earlier = jdx[None, :] < kdx[:, None]
    carry = jnp.where(earlier[None], jnp.exp(jnp.minimum(gaps, 0.0)), 0.0)
    before = jnp.einsum("hkj,jhpn->khpn", carry, block_state, precision=lax.Precision.HIGHEST)
    local_end = before[blocks]
    before = before[:blocks]
    shard_total = jnp.sum(totals, axis=0)

    amax = jnp.max(jnp.abs(local_end), axis=-1, keepdims=True)
    scale = amax / 32767.0
    coded = jnp.clip(
        jnp.round(local_end / jnp.where(scale > 0, scale, 1.0)), -32767.0, 32767.0
    ).astype(jnp.int16)
    side = jnp.concatenate(
        [scale.reshape(-1), shard_total, jnp.zeros((lanes - lheads,), jnp.float32)]
    ).reshape(-1, lanes)
    incoming = jnp.zeros_like(local_end)
    gap = jnp.zeros((lheads,), jnp.float32)
    for d in range(1, nx):
        route = [(i, i + d) for i in range(nx - d)]
        piece = lax.ppermute(coded, "sx", route).astype(jnp.float32)
        got = lax.ppermute(side, "sx", route).reshape(-1)
        piece = piece * got[: lheads * hsize].reshape(lheads, hsize, 1)
        incoming = incoming + jnp.exp(gap)[:, None, None] * piece
        gap = gap + got[lheads * hsize : lheads * hsize + lheads]
    prefix = jnp.cumsum(totals, axis=0) - totals
    before = before + jnp.exp(prefix)[:, :, None, None] * incoming[None]

    carried = jnp.einsum(
        "cin,chpn->cihp", cc.astype(jnp.float32), before, precision=lax.Precision.HIGHEST
    )
    skip = lax.dynamic_slice_in_dim(skip_gain[0], lax.axis_index("sz") * lheads, lheads)
    ys = (
        inner
        + jnp.exp(cum)[..., None] * carried
        + skip[None, None, :, None] * xc.astype(jnp.float32)
    )

    ys = code16(ys, "sz").reshape(nz, rows, local)
    ys = jnp.transpose(ys, (1, 0, 2)).reshape(rows, width)
    gated = ys * jax.nn.silu(zs.astype(jnp.float32))
    normed = (
        gated
        * lax.rsqrt(jnp.mean(gated * gated, axis=-1, keepdims=True) + 1e-05)
        * norm_gain[0][None, :]
    ).astype(jnp.bfloat16)
    mixed = jnp.dot(
        normed,
        lax.all_gather(out_weight[0], SEQ, axis=1, tiled=True),
        preferred_element_type=jnp.float32,
    ).astype(jnp.bfloat16)
    return mixed.reshape(1, rows, mixed.shape[-1])


def solution(mesh):
    shards = mesh.shape["seq"]
    inner = 4 if shards % 4 == 0 else shards
    split = Mesh(
        np.asarray(mesh.devices).reshape(mesh.shape["dom"], shards // inner, inner),
        ("dom",) + SEQ,
    )
    rows = P(("dom",) + SEQ, None)
    in_specs = (
        rows,
        rows,
        rows,
        rows,
        rows,
        P("dom", SEQ, None),
        P("dom", None, SEQ),
        P("dom", None),
        P("dom", None),
    )
    out_specs = P("dom", SEQ, None)
    return jax.shard_map(
        per_device, mesh=split, in_specs=in_specs, out_specs=out_specs, check_vma=False
    )
```

```python
import jax
import jax.numpy as jnp
import numpy as np
from jax import lax
from jax.sharding import Mesh
from jax.sharding import PartitionSpec as P

SPAN = 256
SEQ = ("sx", "sz")


def code16(values, axis_name):
    amax = jnp.max(jnp.abs(values), axis=-1, keepdims=True)
    scale = amax / 32767.0
    coded = jnp.clip(jnp.round(values / jnp.where(scale > 0, scale, 1.0)), -32767.0, 32767.0)
    lead = values.shape[:2]
    coded = lax.all_to_all(
        coded.astype(jnp.int16).reshape(*lead, -1), axis_name, split_axis=0, concat_axis=0, tiled=True
    )
    scale = lax.all_to_all(
        scale.reshape(*lead, -1), axis_name, split_axis=0, concat_axis=0, tiled=True
    )
    return coded.reshape(values.shape).astype(jnp.float32) * scale[..., None]


def per_device(
    tokens_x, gate_z, in_b, in_c, log_decay, domain_ids, out_weight, norm_gain, skip_gain
):
    groups = lax.axis_size("dom")
    nx = lax.axis_size("sx")
    nz = lax.axis_size("sz")
    rows = tokens_x.shape[0]
    seg_rows = rows // groups
    width = tokens_x.shape[1]
    nstate = in_b.shape[1]
    heads = skip_gain.shape[-1]
    hsize = width // heads
    order = jnp.argsort(domain_ids.reshape(groups))

    def arrange(value_rows):
        return jnp.take(value_rows.reshape(groups, seg_rows, value_rows.shape[-1]), order, axis=0)

    local = width // nz
    lheads = heads // nz
    lanes = 128
    xpart = jnp.transpose(arrange(tokens_x).reshape(groups, seg_rows, nz, local), (0, 2, 1, 3))
    side = jnp.broadcast_to(
        arrange(jnp.concatenate([in_b, in_c], axis=1))[:, None], (groups, nz, seg_rows, 2 * nstate)
    )
    routed = jnp.concatenate([xpart, side], axis=3)
    routed = routed.reshape(groups * nz, seg_rows, routed.shape[-1])
    routed = lax.all_to_all(routed, ("dom", "sz"), split_axis=0, concat_axis=0, tiled=True)
    routed = jnp.transpose(routed.reshape(groups, nz, seg_rows, routed.shape[-1]), (1, 0, 2, 3))
    routed = routed.reshape(nz * rows, routed.shape[-1])
    pad = (-log_decay.shape[1]) % lanes
    zl = jnp.concatenate([gate_z, log_decay, jnp.zeros((rows, pad), log_decay.dtype)], axis=1)
    zl = lax.all_to_all(arrange(zl), "dom", split_axis=0, concat_axis=0, tiled=True)
    zl = zl.reshape(rows, zl.shape[-1])
    zs = zl[:, :width]
    lsh = jnp.transpose(zl[:, width : width + heads].reshape(rows, nz, lheads), (1, 0, 2))
    lsh = lax.all_to_all(lsh, "sz", split_axis=0, concat_axis=0, tiled=True)

    blocks = nz * rows // SPAN
    xc = routed[:, :local].reshape(blocks, SPAN, lheads, hsize)
    bc = routed[:, local : local + nstate].reshape(blocks, SPAN, nstate)
    cc = routed[:, local + nstate : local + 2 * nstate].reshape(blocks, SPAN, nstate)
    cum = jnp.cumsum(lsh.astype(jnp.float32).reshape(blocks, SPAN, lheads), axis=1)
    scores = jnp.einsum("cin,cjn->cij", cc, bc, preferred_element_type=jnp.float32)
    cum_heads = jnp.transpose(cum, (0, 2, 1))
    diff = cum_heads[:, :, :, None] - cum_heads[:, :, None, :]
    positions = jnp.arange(SPAN)
    lower = positions[:, None] >= positions[None, :]
    decay = jnp.where(lower[None, None], jnp.exp(jnp.minimum(diff, 0.0)), 0.0)
    weights = (scores[:, None] * decay).astype(jnp.bfloat16)
    inner = jnp.einsum("chij,cjhp->cihp", weights, xc, preferred_element_type=jnp.float32)
    totals = cum[:, -1, :]
    decayed = (xc.astype(jnp.float32) * jnp.exp(totals[:, None, :] - cum)[..., None]).astype(
        jnp.bfloat16
    )
    block_state = jnp.einsum("cjhp,cjn->chpn", decayed, bc, preferred_element_type=jnp.float32)

    kdx = jnp.arange(blocks + 1)
    jdx = jnp.arange(blocks)
    between = (jdx[None, :, None] < jdx[None, None, :]) & (jdx[None, None, :] < kdx[:, None, None])
    gaps = jnp.einsum(
        "kji,ih->hkj", between.astype(jnp.float32), totals, precision=lax.Precision.HIGHEST
    )
    earlier = jdx[None, :] < kdx[:, None]
    carry = jnp.where(earlier[None], jnp.exp(jnp.minimum(gaps, 0.0)), 0.0)
    before = jnp.einsum("hkj,jhpn->khpn", carry, block_state, precision=lax.Precision.HIGHEST)
    local_end = before[blocks]
    before = before[:blocks]
    shard_total = jnp.sum(totals, axis=0)

    amax = jnp.max(jnp.abs(local_end), axis=-1, keepdims=True)
    scale = amax / 32767.0
    coded = jnp.clip(
        jnp.round(local_end / jnp.where(scale > 0, scale, 1.0)), -32767.0, 32767.0
    ).astype(jnp.int16)
    side = jnp.concatenate(
        [scale.reshape(-1), shard_total, jnp.zeros((lanes - lheads,), jnp.float32)]
    ).reshape(-1, lanes)
    incoming = jnp.zeros_like(local_end)
    gap = jnp.zeros((lheads,), jnp.float32)
    for d in range(1, nx):
        route = [(i, i + d) for i in range(nx - d)]
        piece = lax.ppermute(coded, "sx", route).astype(jnp.float32)
        got = lax.ppermute(side, "sx", route).reshape(-1)
        piece = piece * got[: lheads * hsize].reshape(lheads, hsize, 1)
        incoming = incoming + jnp.exp(gap)[:, None, None] * piece
        gap = gap + got[lheads * hsize : lheads * hsize + lheads]
    prefix = jnp.cumsum(totals, axis=0) - totals
    before = before + jnp.exp(prefix)[:, :, None, None] * incoming[None]

    carried = jnp.einsum(
        "cin,chpn->cihp", cc.astype(jnp.float32), before, precision=lax.Precision.HIGHEST
    )
    skip = lax.dynamic_slice_in_dim(skip_gain[0], lax.axis_index("sz") * lheads, lheads)
    ys = (
        inner
        + jnp.exp(cum)[..., None] * carried
        + skip[None, None, :, None] * xc.astype(jnp.float32)
    )

    ys = code16(ys, "sz").reshape(nz, rows, local)
    ys = jnp.transpose(ys, (1, 0, 2)).reshape(rows, width)
    gated = ys * jax.nn.silu(zs.astype(jnp.float32))
    normed = (
        gated
        * lax.rsqrt(jnp.mean(gated * gated, axis=-1, keepdims=True) + 1e-05)
        * norm_gain[0][None, :]
    ).astype(jnp.bfloat16)
    mixed = jnp.dot(
        normed,
        lax.all_gather(out_weight[0], SEQ, axis=1, tiled=True),
        preferred_element_type=jnp.float32,
    ).astype(jnp.bfloat16)
    return mixed.reshape(1, rows, mixed.shape[-1])


def solution(mesh):
    shards = mesh.shape["seq"]
    inner = 4 if shards % 4 == 0 else shards
    split = Mesh(
        np.asarray(mesh.devices).reshape(mesh.shape["dom"], shards // inner, inner),
        ("dom",) + SEQ,
    )
    rows = P(("dom",) + SEQ, None)
    in_specs = (
        rows,
        rows,
        rows,
        rows,
        rows,
        P("dom", SEQ, None),
        P("dom", None, SEQ),
        P("dom", None),
        P("dom", None),
    )
    out_specs = P("dom", SEQ, None)
    return jax.shard_map(
        per_device, mesh=split, in_specs=in_specs, out_specs=out_specs, check_vma=False
    )
```

```python
import jax
import jax.numpy as jnp
import numpy as np
from jax import lax
from jax.sharding import Mesh
from jax.sharding import PartitionSpec as P

SPAN = 256
SEQ = ("sx", "sz")


def code16(values, axis_name):
    amax = jnp.max(jnp.abs(values), axis=-1, keepdims=True)
    scale = amax / 32767.0
    coded = jnp.clip(jnp.round(values / jnp.where(scale > 0, scale, 1.0)), -32767.0, 32767.0)
    lead = values.shape[:2]
    coded = lax.all_to_all(
        coded.astype(jnp.int16).reshape(*lead, -1), axis_name, split_axis=0, concat_axis=0, tiled=True
    )
    scale = lax.all_to_all(
        scale.reshape(*lead, -1), axis_name, split_axis=0, concat_axis=0, tiled=True
    )
    return coded.reshape(values.shape).astype(jnp.float32) * scale[..., None]


def per_device(
    tokens_x, gate_z, in_b, in_c, log_decay, domain_ids, out_weight, norm_gain, skip_gain
):
    groups = lax.axis_size("dom")
    nx = lax.axis_size("sx")
    nz = lax.axis_size("sz")
    rows = tokens_x.shape[0]
    seg_rows = rows // groups
    width = tokens_x.shape[1]
    nstate = in_b.shape[1]
    heads = skip_gain.shape[-1]
    hsize = width // heads
    order = jnp.argsort(domain_ids.reshape(groups))

    def arrange(value_rows):
        return jnp.take(value_rows.reshape(groups, seg_rows, value_rows.shape[-1]), order, axis=0)

    local = width // nz
    lheads = heads // nz
    lanes = 128
    xpart = jnp.transpose(arrange(tokens_x).reshape(groups, seg_rows, nz, local), (0, 2, 1, 3))
    side = jnp.broadcast_to(
        arrange(jnp.concatenate([in_b, in_c], axis=1))[:, None], (groups, nz, seg_rows, 2 * nstate)
    )
    routed = jnp.concatenate([xpart, side], axis=3)
    routed = routed.reshape(groups * nz, seg_rows, routed.shape[-1])
    routed = lax.all_to_all(routed, ("dom", "sz"), split_axis=0, concat_axis=0, tiled=True)
    routed = jnp.transpose(routed.reshape(groups, nz, seg_rows, routed.shape[-1]), (1, 0, 2, 3))
    routed = routed.reshape(nz * rows, routed.shape[-1])
    pad = (-log_decay.shape[1]) % lanes
    zl = jnp.concatenate([gate_z, log_decay, jnp.zeros((rows, pad), log_decay.dtype)], axis=1)
    zl = lax.all_to_all(arrange(zl), "dom", split_axis=0, concat_axis=0, tiled=True)
    zl = zl.reshape(rows, zl.shape[-1])
    zs = zl[:, :width]
    lsh = jnp.transpose(zl[:, width : width + heads].reshape(rows, nz, lheads), (1, 0, 2))
    lsh = lax.all_to_all(lsh, "sz", split_axis=0, concat_axis=0, tiled=True)

    blocks = nz * rows // SPAN
    xc = routed[:, :local].reshape(blocks, SPAN, lheads, hsize)
    bc = routed[:, local : local + nstate].reshape(blocks, SPAN, nstate)
    cc = routed[:, local + nstate : local + 2 * nstate].reshape(blocks, SPAN, nstate)
    cum = jnp.cumsum(lsh.astype(jnp.float32).reshape(blocks, SPAN, lheads), axis=1)
    scores = jnp.einsum("cin,cjn->cij", cc, bc, preferred_element_type=jnp.float32)
    cum_heads = jnp.transpose(cum, (0, 2, 1))
    diff = cum_heads[:, :, :, None] - cum_heads[:, :, None, :]
    positions = jnp.arange(SPAN)
    lower = positions[:, None] >= positions[None, :]
    decay = jnp.where(lower[None, None], jnp.exp(jnp.minimum(diff, 0.0)), 0.0)
    weights = (scores[:, None] * decay).astype(jnp.bfloat16)
    inner = jnp.einsum("chij,cjhp->cihp", weights, xc, preferred_element_type=jnp.float32)
    totals = cum[:, -1, :]
    decayed = (xc.astype(jnp.float32) * jnp.exp(totals[:, None, :] - cum)[..., None]).astype(
        jnp.bfloat16
    )
    block_state = jnp.einsum("cjhp,cjn->chpn", decayed, bc, preferred_element_type=jnp.float32)

    kdx = jnp.arange(blocks + 1)
    jdx = jnp.arange(blocks)
    between = (jdx[None, :, None] < jdx[None, None, :]) & (jdx[None, None, :] < kdx[:, None, None])
    gaps = jnp.einsum(
        "kji,ih->hkj", between.astype(jnp.float32), totals, precision=lax.Precision.HIGHEST
    )
    earlier = jdx[None, :] < kdx[:, None]
    carry = jnp.where(earlier[None], jnp.exp(jnp.minimum(gaps, 0.0)), 0.0)
    before = jnp.einsum("hkj,jhpn->khpn", carry, block_state, precision=lax.Precision.HIGHEST)
    local_end = before[blocks]
    before = before[:blocks]
    shard_total = jnp.sum(totals, axis=0)

    amax = jnp.max(jnp.abs(local_end), axis=-1, keepdims=True)
    scale = amax / 32767.0
    coded = jnp.clip(
        jnp.round(local_end / jnp.where(scale > 0, scale, 1.0)), -32767.0, 32767.0
    ).astype(jnp.int16)
    side = jnp.concatenate(
        [scale.reshape(-1), shard_total, jnp.zeros((lanes - lheads,), jnp.float32)]
    ).reshape(-1, lanes)
    incoming = jnp.zeros_like(local_end)
    gap = jnp.zeros((lheads,), jnp.float32)
    for d in range(1, nx):
        route = [(i, i + d) for i in range(nx - d)]
        piece = lax.ppermute(coded, "sx", route).astype(jnp.float32)
        got = lax.ppermute(side, "sx", route).reshape(-1)
        piece = piece * got[: lheads * hsize].reshape(lheads, hsize, 1)
        incoming = incoming + jnp.exp(gap)[:, None, None] * piece
        gap = gap + got[lheads * hsize : lheads * hsize + lheads]
    prefix = jnp.cumsum(totals, axis=0) - totals
    before = before + jnp.exp(prefix)[:, :, None, None] * incoming[None]

    carried = jnp.einsum(
        "cin,chpn->cihp", cc.astype(jnp.float32), before, precision=lax.Precision.HIGHEST
    )
    skip = lax.dynamic_slice_in_dim(skip_gain[0], lax.axis_index("sz") * lheads, lheads)
    ys = (
        inner
        + jnp.exp(cum)[..., None] * carried
        + skip[None, None, :, None] * xc.astype(jnp.float32)
    )

    ys = code16(ys, "sz").reshape(nz, rows, local)
    ys = jnp.transpose(ys, (1, 0, 2)).reshape(rows, width)
    gated = ys * jax.nn.silu(zs.astype(jnp.float32))
    normed = (
        gated
        * lax.rsqrt(jnp.mean(gated * gated, axis=-1, keepdims=True) + 1e-05)
        * norm_gain[0][None, :]
    ).astype(jnp.bfloat16)
    normed = lax.optimization_barrier(normed)
    mixed = jnp.dot(
        normed,
        lax.all_gather(out_weight[0], SEQ, axis=1, tiled=True),
        preferred_element_type=jnp.float32,
    ).astype(jnp.bfloat16)
    return mixed.reshape(1, rows, mixed.shape[-1])


def solution(mesh):
    shards = mesh.shape["seq"]
    inner = 4 if shards % 4 == 0 else shards
    split = Mesh(
        np.asarray(mesh.devices).reshape(mesh.shape["dom"], shards // inner, inner),
        ("dom",) + SEQ,
    )
    rows = P(("dom",) + SEQ, None)
    in_specs = (
        rows,
        rows,
        rows,
        rows,
        rows,
        P("dom", SEQ, None),
        P("dom", None, SEQ),
        P("dom", None),
        P("dom", None),
    )
    out_specs = P("dom", SEQ, None)
    return jax.shard_map(
        per_device, mesh=split, in_specs=in_specs, out_specs=out_specs, check_vma=False
    )
```
